128 devices in a mesh: dom: 16 (over x, z), outer: 8 (over y, core).
Axes of the slice: x: 4, y: 4, z: 4, core: 2. Of those that a mesh axis runs over, the one named last changes fastest.
Arguments:
- jacobian: bfloat16 [16384, 7, 4096], P(('dom', 'outer')), may hold values from -0.25 to 0.25
- pod_basis: bfloat16 [16384, 4096], P(('dom', 'outer')), may hold values from -6 to 6
- ghost_rows: int32 [128, 128, 4], P(None, ('dom', 'outer')), may hold values from 0 to 127, as said below
- column_slot: int32 [16384, 7], P(('dom', 'outer')), may hold values from -1 to 511, as said below
Outputs:
- galerkin_rows: bfloat16 [16384, 4096], P(('dom', 'outer'))
- reduced: float32 [64, 64], replicated
The draws below stay inside these ranges and needn't reach their ends.
Inputs may be any that keep to these rules, and one draw needn't show every extreme that they name: `ghost_rows`: each list has 4 entries, repeats allowed. `column_slot`: slot 0 holds the block row's diagonal block. Slots 0 to 3 are always used, and over the rows of one device they name every table entry exactly once. Slots 4 to 6 may be unused (-1); unused slots come after all used ones; some rows use all 7 slots and some only four.
All inputs are finite; a program needn't handle non-finite values.
Results may differ from the reference program's by a relative error of at most 0.003.
Values may be sent and summed in bfloat16 or wider, within the bound.
No kernel may reach another device: no remote copies, remote signals or barrier semaphores. Data moves between devices by JAX's collectives and lax.ppermute only.
A program may use at most 128 MiB of HBM per device.

```python
import math
import jax
import jax.numpy as jnp
from jax import lax

BLOCK = 64
MODES = 64
SLOTS = 7
ROWS_DEV = 128
GHOSTS = 4
NBLOCKS = 16384
DEVICES = 128


def draw_ghost_rows(key, part):
    values = jax.random.randint(key, (DEVICES, DEVICES, GHOSTS), 0, ROWS_DEV, dtype=jnp.int32)
    values = values.at[0, 0, 0].set(ROWS_DEV - 1)
    values = values.at[DEVICES - 1, DEVICES - 2, GHOSTS - 1].set(0)
    return values


def draw_column_slot(key, part):
    entries = DEVICES * GHOSTS
    perm_key = jax.random.fold_in(key, 11)
    extra_key = jax.random.fold_in(key, 12)
    count_key = jax.random.fold_in(key, 13)
    device_keys = jax.random.split(perm_key, DEVICES)
    orders = jax.vmap(lambda single: jax.random.permutation(single, entries))(device_keys)
    first_four = orders.astype(jnp.int32).reshape(DEVICES, 4, ROWS_DEV).transpose(0, 2, 1)
    extra = jax.random.randint(extra_key, (DEVICES, ROWS_DEV, SLOTS - 4), 0, entries, dtype=jnp.int32)
    counts = jax.random.randint(count_key, (DEVICES, ROWS_DEV), 4, SLOTS + 1, dtype=jnp.int32)
    counts = counts.at[:, 0].set(SLOTS).at[:, 1].set(4)
    positions = jnp.arange(SLOTS - 4, dtype=jnp.int32) + 4
    extra = jnp.where(positions[None, None, :] < counts[:, :, None], extra, -1)
    slots = jnp.concatenate([first_four, extra], axis=2)
    return slots.reshape(NBLOCKS, SLOTS)


def block_scale(own_key, shape, pieces, smallest, top_value):
    def one(position, parts):
        heights = jax.random.uniform(jax.random.fold_in(jax.random.fold_in(own_key, 6), position), (parts,), jnp.float32, smallest / len(pieces), top_value / len(pieces))
        return jnp.repeat(jnp.exp(heights), shape[position] // parts).reshape((-1,) + (1,) * (len(shape) - position - 1))

    factor_of = one(*pieces[0])
    for cut in pieces[1:]:
        factor_of = factor_of * one(*cut)
    return factor_of


def gaussian(rng, shape, width, bound, pieces=(), held_as=jnp.bfloat16):
    result = width * jax.random.normal(rng, shape, jnp.float32)
    if pieces:
        result = result * block_scale(rng, shape, pieces, -0.22, 0.18)
    return jnp.clip(result, -bound, bound).astype(held_as)


def setup_inputs(seed: int = 0) -> dict:
    arg_keys = jax.random.split(jax.random.key(seed), 5)
    jacobian = gaussian(arg_keys[0], (NBLOCKS, SLOTS, BLOCK * BLOCK), (BLOCK * SLOTS) ** -0.5, 0.25, ((0, 128),))
    pod_basis = gaussian(arg_keys[1], (NBLOCKS, BLOCK * MODES), 1.0, 6.0, ((0, 128),))
    ghost_rows = draw_ghost_rows(jax.random.fold_in(arg_keys[4], 71), 0)
    column_slot = draw_column_slot(jax.random.fold_in(arg_keys[4], 71), 0)
    return {"jacobian": jacobian, "pod_basis": pod_basis, "ghost_rows": ghost_rows, "column_slot": column_slot}


def reference(jacobian, pod_basis, ghost_rows, column_slot):

    def per_device(device):
        ghost_lists = ghost_rows[device]
        global_rows = (jnp.arange(DEVICES, dtype=jnp.int32)[:, None] * ROWS_DEV + ghost_lists).reshape(-1)
        lookup = pod_basis[global_rows].astype(jnp.float32).reshape(-1, BLOCK, MODES)
        start = (device * ROWS_DEV).astype(jnp.int32)
        jac_blocks = lax.dynamic_slice_in_dim(jacobian, start, ROWS_DEV, 0).astype(jnp.float32)
        jac_blocks = jac_blocks.reshape(ROWS_DEV, SLOTS, BLOCK, BLOCK)
        slot_index = lax.dynamic_slice_in_dim(column_slot, start, ROWS_DEV, 0)
        live_slot = (slot_index >= 0).astype(jnp.float32)
        picked = lookup[jnp.maximum(slot_index, 0)] * live_slot[:, :, None, None]
        products = jnp.einsum('rsij,rsjk->rik', jac_blocks, picked, precision=lax.Precision.HIGHEST)
        rounded = lax.optimization_barrier(products.astype(jnp.bfloat16))
        diag_rows = lookup[slot_index[:, 0]]
        partial_value = jnp.einsum('rik,ril->kl', diag_rows, rounded.astype(jnp.float32), precision=lax.Precision.HIGHEST)
        return (rounded.reshape(ROWS_DEV, BLOCK * MODES), partial_value)
    row_blocks, partials = lax.map(per_device, jnp.arange(DEVICES, dtype=jnp.int32))
    galerkin_rows = row_blocks.reshape(NBLOCKS, BLOCK * MODES)
    reduced = lax.optimization_barrier(jnp.sum(partials, axis=0)) / math.sqrt(NBLOCKS * BLOCK)
    return (galerkin_rows, reduced)
```

```python
import math

import jax
import jax.numpy as jnp
from jax import lax
from jax.sharding import PartitionSpec as P

BLOCK = 64
MODES = 64
SLOTS = 7


def on_device(jacobian, pod_basis, ghost_rows, column_slot):
    rows_local = pod_basis.shape[0]
    block_area = pod_basis.shape[1]
    dom_count = lax.axis_size("dom")
    outer_count = lax.axis_size("outer")
    device_count = dom_count * outer_count
    ghost_lists = ghost_rows[:, 0, :]
    ghost_count = ghost_lists.shape[1]
    chooser = jax.nn.one_hot(ghost_lists.reshape(-1), rows_local, dtype=jnp.bfloat16)
    outgoing = jnp.dot(chooser, pod_basis, preferred_element_type=jnp.float32).astype(jnp.bfloat16)
    outgoing = outgoing.reshape(device_count, ghost_count, block_area)
    received = lax.all_to_all(outgoing, ("dom", "outer"), split_axis=0, concat_axis=0, tiled=True)
    table = received.reshape(device_count * ghost_count, block_area)
    entries = table.shape[0]
    products = jnp.zeros((rows_local, BLOCK, MODES), jnp.float32)
    diag_rows = None
    for slot in range(SLOTS):
        selector = jax.nn.one_hot(column_slot[:, slot], entries, dtype=jnp.bfloat16)
        picked = jnp.dot(selector, table, preferred_element_type=jnp.float32).astype(jnp.bfloat16)
        picked = picked.reshape(rows_local, BLOCK, MODES)
        if slot == 0:
            diag_rows = picked
        jac_slot = jacobian[:, slot, :].reshape(rows_local, BLOCK, BLOCK)
        products = products + jnp.einsum(
            "rij,rjk->rik", jac_slot, picked, preferred_element_type=jnp.float32
        )
    rounded = products.astype(jnp.bfloat16)
    partial_value = jnp.einsum(
        "rik,ril->kl", diag_rows, rounded, preferred_element_type=jnp.float32
    )
    total = partial_value
    for bit in range(device_count.bit_length() - 1):
        pairs = [(i, i ^ (1 << bit)) for i in range(device_count)]
        total = total + lax.ppermute(total, ("dom", "outer"), pairs)
    reduced = total / math.sqrt(rows_local * device_count * BLOCK)
    galerkin_rows = rounded.reshape(rows_local, block_area)
    return (galerkin_rows, reduced)


def solution(mesh):
    placed = (
        P(("dom", "outer"), None, None),
        P(("dom", "outer"), None),
        P(None, ("dom", "outer"), None),
        P(("dom", "outer"), None),
    )
    return jax.shard_map(
        on_device,
        mesh=mesh,
        in_specs=placed,
        out_specs=(P(("dom", "outer"), None), P()),
        check_vma=False,
    )
```

```python
import math

import jax
import jax.numpy as jnp
from jax import lax
from jax.experimental import pallas as pl
from jax.experimental.pallas import tpu as pltpu
from jax.sharding import PartitionSpec as P

BLOCK = 64
MODES = 64
SLOTS = 7
ROW_TILE = 16


def gather_outgoing(pod_basis, picks):
    rows_local, block_area = pod_basis.shape
    count = picks.shape[0]
    sub = block_area // 128

    def body(pick_ref, pod_ref, out_ref, slab_ref):
        slab_ref[...] = pod_ref[...].reshape(rows_local, sub, 128)

        def one(n, carry):
            out_ref[n] = slab_ref[pick_ref[n]]
            return carry

        lax.fori_loop(0, count, one, 0)

    grid_spec = pltpu.PrefetchScalarGridSpec(
        num_scalar_prefetch=1,
        grid=(1,),
        in_specs=[pl.BlockSpec((rows_local, block_area), lambda i, p: (0, 0))],
        out_specs=pl.BlockSpec((count, sub, 128), lambda i, p: (0, 0, 0)),
        scratch_shapes=[pltpu.VMEM((rows_local, sub, 128), pod_basis.dtype)],
    )
    return pl.pallas_call(
        body,
        grid_spec=grid_spec,
        out_shape=jax.ShapeDtypeStruct((count, sub, 128), pod_basis.dtype),
    )(picks, pod_basis)


def block_products(jac_by_slot, table, column_slot):
    slots, rows, block_area = jac_by_slot.shape
    entries = table.shape[0]
    tile = ROW_TILE
    flat_slots = column_slot.reshape(-1)

    def body(col_ref, jac_ref, tab_ref, out_ref, part_ref):
        step = pl.program_id(0)
        acc = jnp.zeros((tile, BLOCK, MODES), jnp.float32)
        diag = None
        for j in range(slots):
            lhs = jac_ref[j].reshape(tile, BLOCK, BLOCK)
            picked = []
            for r in range(tile):
                e = col_ref[(step * tile + r) * slots + j]
                blk = tab_ref[jnp.maximum(e, 0)]
                picked.append(jnp.where(e >= 0, blk, jnp.zeros_like(blk)))
            rhs = jnp.stack(picked).reshape(tile, BLOCK, MODES)
            if j == 0:
                diag = rhs
            acc = acc + jnp.einsum(
                "rik,rkm->rim", lhs, rhs, preferred_element_type=jnp.float32
            )
        rounded = acc.astype(jnp.bfloat16)
        out_ref[...] = rounded.reshape(tile, block_area)
        contrib = lax.dot_general(
            diag.reshape(tile * BLOCK, MODES),
            rounded.reshape(tile * BLOCK, MODES),
            (((0,), (0,)), ((), ())),
            preferred_element_type=jnp.float32,
        )

        @pl.when(step == 0)
        def _():
            part_ref[...] = jnp.zeros_like(part_ref)

        part_ref[...] += contrib

    grid_spec = pltpu.PrefetchScalarGridSpec(
        num_scalar_prefetch=1,
        grid=(rows // tile,),
        in_specs=[
            pl.BlockSpec((slots, tile, block_area), lambda i, c: (0, i, 0)),
            pl.BlockSpec(table.shape, lambda i, c: (0, 0, 0)),
        ],
        out_specs=[
            pl.BlockSpec((tile, block_area), lambda i, c: (i, 0)),
            pl.BlockSpec((MODES, MODES), lambda i, c: (0, 0)),
        ],
    )
    return pl.pallas_call(
        body,
        grid_spec=grid_spec,
        out_shape=(
            jax.ShapeDtypeStruct((rows, block_area), jnp.bfloat16),
            jax.ShapeDtypeStruct((MODES, MODES), jnp.float32),
        ),
        compiler_params=pltpu.CompilerParams(dimension_semantics=("arbitrary",)),
    )(flat_slots, jac_by_slot, table)


def on_device(jacobian, pod_basis, ghost_rows, column_slot):
    rows_local = pod_basis.shape[0]
    dom_count = lax.axis_size("dom")
    outer_count = lax.axis_size("outer")
    device_count = dom_count * outer_count
    ghost_lists = ghost_rows[:, 0, :]
    ghost_count = ghost_lists.shape[1]
    outgoing = gather_outgoing(pod_basis, ghost_lists.reshape(-1))
    outgoing = outgoing.reshape((device_count, ghost_count) + outgoing.shape[1:])
    received = lax.all_to_all(outgoing, ("dom", "outer"), split_axis=0, concat_axis=0, tiled=True)
    table = received.reshape((device_count * ghost_count,) + received.shape[2:])
    jac_by_slot = jnp.transpose(jacobian, (1, 0, 2))
    galerkin_rows, partial_value = block_products(jac_by_slot, table, column_slot)
    total = partial_value
    for bit in range(device_count.bit_length() - 1):
        pairs = [(i, i ^ (1 << bit)) for i in range(device_count)]
        total = total + lax.ppermute(total, ("dom", "outer"), pairs)
    reduced = total / math.sqrt(rows_local * device_count * BLOCK)
    return (galerkin_rows, reduced)


def solution(mesh):
    placed = (
        P(("dom", "outer"), None, None),
        P(("dom", "outer"), None),
        P(None, ("dom", "outer"), None),
        P(("dom", "outer"), None),
    )
    return jax.shard_map(
        on_device,
        mesh=mesh,
        in_specs=placed,
        out_specs=(P(("dom", "outer"), None), P()),
        check_vma=False,
    )
```

```python
import math

import jax
import jax.numpy as jnp
from jax import lax
from jax.experimental import pallas as pl
from jax.experimental.pallas import tpu as pltpu
from jax.sharding import PartitionSpec as P

BLOCK = 64
MODES = 64
SLOTS = 7
ROW_TILE = 16


def gather_outgoing(pod_basis, picks):
    rows_local, block_area = pod_basis.shape
    count = picks.shape[0]
    sub = block_area // 128

    def body(pick_ref, pod_ref, out_ref, slab_ref):
        slab_ref[...] = pod_ref[...].reshape(rows_local, sub, 128)

        def one(n, carry):
            out_ref[n] = slab_ref[pick_ref[n]]
            return carry

        lax.fori_loop(0, count, one, 0, unroll=8)

    grid_spec = pltpu.PrefetchScalarGridSpec(
        num_scalar_prefetch=1,
        grid=(1,),
        in_specs=[pl.BlockSpec((rows_local, block_area), lambda i, p: (0, 0))],
        out_specs=pl.BlockSpec((count, sub, 128), lambda i, p: (0, 0, 0)),
        scratch_shapes=[pltpu.VMEM((rows_local, sub, 128), pod_basis.dtype)],
    )
    return pl.pallas_call(
        body,
        grid_spec=grid_spec,
        out_shape=jax.ShapeDtypeStruct((count, sub, 128), pod_basis.dtype),
    )(picks, pod_basis)


def block_products(jac_by_slot, table, column_slot):
    slots, rows, block_area = jac_by_slot.shape
    entries = table.shape[0]
    tile = ROW_TILE
    flat_slots = column_slot.reshape(-1)

    def body(col_ref, jac_ref, tab_ref, out_ref, part_ref, blocks_ref):
        step = pl.program_id(0)

        @pl.when(step == 0)
        def _():
            def relayout(c, carry):
                chunk = pl.ds(c * tile, tile)
                blocks_ref[chunk] = tab_ref[chunk].reshape(tile, BLOCK, MODES)
                return carry

            lax.fori_loop(0, entries // tile, relayout, 0)
            blocks_ref[entries] = jnp.zeros((BLOCK, MODES), blocks_ref.dtype)
            part_ref[...] = jnp.zeros_like(part_ref)

        acc = jnp.zeros((tile, BLOCK, MODES), jnp.float32)
        diag = None
        for j in range(slots):
            lhs = jac_ref[j].reshape(tile, BLOCK, BLOCK)
            picked = []
            for r in range(tile):
                e = col_ref[(step * tile + r) * slots + j]
                picked.append(blocks_ref[jnp.where(e >= 0, e, entries)])
            rhs = jnp.stack(picked)
            if j == 0:
                diag = rhs
            acc = acc + jnp.einsum(
                "rik,rkm->rim", lhs, rhs, preferred_element_type=jnp.float32
            )
        rounded = acc.astype(jnp.bfloat16)
        out_ref[...] = rounded.reshape(tile, block_area)
        part_ref[...] += lax.dot_general(
            diag.reshape(tile * BLOCK, MODES),
            rounded.reshape(tile * BLOCK, MODES),
            (((0,), (0,)), ((), ())),
            preferred_element_type=jnp.float32,
        )

    grid_spec = pltpu.PrefetchScalarGridSpec(
        num_scalar_prefetch=1,
        grid=(rows // tile,),
        in_specs=[
            pl.BlockSpec((slots, tile, block_area), lambda i, c: (0, i, 0)),
            pl.BlockSpec(table.shape, lambda i, c: (0, 0, 0)),
        ],
        out_specs=[
            pl.BlockSpec((tile, block_area), lambda i, c: (i, 0)),
            pl.BlockSpec((MODES, MODES), lambda i, c: (0, 0)),
        ],
        scratch_shapes=[pltpu.VMEM((entries + 1, BLOCK, MODES), table.dtype)],
    )
    return pl.pallas_call(
        body,
        grid_spec=grid_spec,
        out_shape=(
            jax.ShapeDtypeStruct((rows, block_area), jnp.bfloat16),
            jax.ShapeDtypeStruct((MODES, MODES), jnp.float32),
        ),
        compiler_params=pltpu.CompilerParams(dimension_semantics=("arbitrary",)),
    )(flat_slots, jac_by_slot, table)


def on_device(jacobian, pod_basis, ghost_rows, column_slot):
    rows_local = pod_basis.shape[0]
    dom_count = lax.axis_size("dom")
    outer_count = lax.axis_size("outer")
    device_count = dom_count * outer_count
    ghost_lists = ghost_rows[:, 0, :]
    ghost_count = ghost_lists.shape[1]
    outgoing = gather_outgoing(pod_basis, ghost_lists.reshape(-1))
    outgoing = outgoing.reshape((device_count, ghost_count) + outgoing.shape[1:])
    received = lax.all_to_all(outgoing, ("dom", "outer"), split_axis=0, concat_axis=0, tiled=True)
    table = received.reshape((device_count * ghost_count,) + received.shape[2:])
    jac_by_slot = jnp.transpose(jacobian, (1, 0, 2))
    galerkin_rows, partial_value = block_products(jac_by_slot, table, column_slot)
    total = partial_value
    for bit in range(device_count.bit_length() - 1):
        pairs = [(i, i ^ (1 << bit)) for i in range(device_count)]
        total = total + lax.ppermute(total, ("dom", "outer"), pairs)
    reduced = total / math.sqrt(rows_local * device_count * BLOCK)
    return (galerkin_rows, reduced)


def solution(mesh):
    placed = (
        P(("dom", "outer"), None, None),
        P(("dom", "outer"), None),
        P(None, ("dom", "outer"), None),
        P(("dom", "outer"), None),
    )
    return jax.shard_map(
        on_device,
        mesh=mesh,
        in_specs=placed,
        out_specs=(P(("dom", "outer"), None), P()),
        check_vma=False,
    )
```

```python
import math

import jax
import jax.numpy as jnp
from jax import lax
from jax.experimental import pallas as pl
from jax.experimental.pallas import tpu as pltpu
from jax.sharding import PartitionSpec as P

BLOCK = 64
MODES = 64
SLOTS = 7
ROW_TILE = 32
SEND_STEPS = 4


def gather_outgoing(pod_basis, picks):
    rows_local, block_area = pod_basis.shape
    count = picks.shape[0]
    sub = block_area // 128

    per_step = count // SEND_STEPS

    def body(pick_ref, pod_ref, out_ref, slab_ref):
        step = pl.program_id(0)

        @pl.when(step == 0)
        def _():
            slab_ref[...] = pod_ref[...].reshape(rows_local, sub, 128)

        def one(n, carry):
            out_ref[n] = slab_ref[pick_ref[step * per_step + n]]
            return carry

        lax.fori_loop(0, per_step, one, 0, unroll=8)

    grid_spec = pltpu.PrefetchScalarGridSpec(
        num_scalar_prefetch=1,
        grid=(SEND_STEPS,),
        in_specs=[pl.BlockSpec((rows_local, block_area), lambda i, p: (0, 0))],
        out_specs=pl.BlockSpec((per_step, sub, 128), lambda i, p: (i, 0, 0)),
        scratch_shapes=[pltpu.VMEM((rows_local, sub, 128), pod_basis.dtype)],
    )
    return pl.pallas_call(
        body,
        grid_spec=grid_spec,
        out_shape=jax.ShapeDtypeStruct((count, sub, 128), pod_basis.dtype),
        compiler_params=pltpu.CompilerParams(dimension_semantics=("arbitrary",)),
    )(picks, pod_basis)


def block_products(jac_by_slot, table, column_slot):
    slots, rows, block_area = jac_by_slot.shape
    entries = table.shape[0]
    tile = ROW_TILE
    flat_slots = column_slot.reshape(-1)

    def body(col_ref, jac_ref, tab_ref, out_ref, part_ref, blocks_ref):
        step = pl.program_id(0)

        @pl.when(step == 0)
        def _():
            def relayout(c, carry):
                chunk = pl.ds(c * tile, tile)
                blocks_ref[chunk] = tab_ref[chunk].reshape(tile, BLOCK, MODES)
                return carry

            lax.fori_loop(0, entries // tile, relayout, 0)
            blocks_ref[entries] = jnp.zeros((BLOCK, MODES), blocks_ref.dtype)
            part_ref[...] = jnp.zeros_like(part_ref)

        acc = jnp.zeros((tile, BLOCK, MODES), jnp.float32)
        diag = None
        for j in range(slots):
            lhs = jac_ref[j].reshape(tile, BLOCK, BLOCK)
            picked = []
            for r in range(tile):
                e = col_ref[(step * tile + r) * slots + j]
                picked.append(blocks_ref[jnp.where(e >= 0, e, entries)])
            rhs = jnp.stack(picked)
            if j == 0:
                diag = rhs
            acc = acc + jnp.einsum(
                "rik,rkm->rim", lhs, rhs, preferred_element_type=jnp.float32
            )
        rounded = acc.astype(jnp.bfloat16)
        out_ref[...] = rounded.reshape(tile, block_area)
        part_ref[...] += lax.dot_general(
            diag.reshape(tile * BLOCK, MODES),
            rounded.reshape(tile * BLOCK, MODES),
            (((0,), (0,)), ((), ())),
            preferred_element_type=jnp.float32,
        )

    grid_spec = pltpu.PrefetchScalarGridSpec(
        num_scalar_prefetch=1,
        grid=(rows // tile,),
        in_specs=[
            pl.BlockSpec((slots, tile, block_area), lambda i, c: (0, i, 0)),
            pl.BlockSpec(table.shape, lambda i, c: (0, 0, 0)),
        ],
        out_specs=[
            pl.BlockSpec((tile, block_area), lambda i, c: (i, 0)),
            pl.BlockSpec((MODES, MODES), lambda i, c: (0, 0)),
        ],
        scratch_shapes=[pltpu.VMEM((entries + 1, BLOCK, MODES), table.dtype)],
    )
    return pl.pallas_call(
        body,
        grid_spec=grid_spec,
        out_shape=(
            jax.ShapeDtypeStruct((rows, block_area), jnp.bfloat16),
            jax.ShapeDtypeStruct((MODES, MODES), jnp.float32),
        ),
        compiler_params=pltpu.CompilerParams(dimension_semantics=("arbitrary",)),
    )(flat_slots, jac_by_slot, table)


def on_device(jacobian, pod_basis, ghost_rows, column_slot):
    rows_local = pod_basis.shape[0]
    dom_count = lax.axis_size("dom")
    outer_count = lax.axis_size("outer")
    device_count = dom_count * outer_count
    ghost_lists = ghost_rows[:, 0, :]
    ghost_count = ghost_lists.shape[1]
    outgoing = gather_outgoing(pod_basis, ghost_lists.reshape(-1))
    outgoing = outgoing.reshape((device_count, ghost_count) + outgoing.shape[1:])
    received = lax.all_to_all(outgoing, ("dom", "outer"), split_axis=0, concat_axis=0, tiled=True)
    table = received.reshape((device_count * ghost_count,) + received.shape[2:])
    jac_by_slot = jnp.transpose(jacobian, (1, 0, 2))
    galerkin_rows, partial_value = block_products(jac_by_slot, table, column_slot)
    total = partial_value
    for bit in range(device_count.bit_length() - 1):
        pairs = [(i, i ^ (1 << bit)) for i in range(device_count)]
        total = total + lax.ppermute(total, ("dom", "outer"), pairs)
    reduced = total / math.sqrt(rows_local * device_count * BLOCK)
    return (galerkin_rows, reduced)


def solution(mesh):
    placed = (
        P(("dom", "outer"), None, None),
        P(("dom", "outer"), None),
        P(None, ("dom", "outer"), None),
        P(("dom", "outer"), None),
    )
    return jax.shard_map(
        on_device,
        mesh=mesh,
        in_specs=placed,
        out_specs=(P(("dom", "outer"), None), P()),
        check_vma=False,
    )
```

```python
import math

import jax
import jax.numpy as jnp
from jax import lax
from jax.experimental import pallas as pl
from jax.experimental.pallas import tpu as pltpu
from jax.sharding import PartitionSpec as P

BLOCK = 64
MODES = 64
SLOTS = 7
ROW_TILE = 32
SEND_STEPS = 4


def gather_outgoing(pod_basis, picks_by_ghost):
    rows_local, block_area = pod_basis.shape
    ghosts, dests = picks_by_ghost.shape
    count = ghosts * dests
    picks = picks_by_ghost.reshape(-1)
    sub = block_area // 128

    per_step = count // SEND_STEPS

    def body(pick_ref, pod_ref, out_ref, slab_ref):
        step = pl.program_id(0)

        @pl.when(step == 0)
        def _():
            slab_ref[...] = pod_ref[...].reshape(rows_local, sub, 128)

        def one(n, carry):
            n_all = step * per_step + n
            out_ref[n] = slab_ref[pick_ref[(n_all % ghosts) * dests + n_all // ghosts]]
            return carry

        lax.fori_loop(0, per_step, one, 0, unroll=8)

    grid_spec = pltpu.PrefetchScalarGridSpec(
        num_scalar_prefetch=1,
        grid=(SEND_STEPS,),
        in_specs=[pl.BlockSpec((rows_local, block_area), lambda i, p: (0, 0))],
        out_specs=pl.BlockSpec((per_step, sub, 128), lambda i, p: (i, 0, 0)),
        scratch_shapes=[pltpu.VMEM((rows_local, sub, 128), pod_basis.dtype)],
    )
    return pl.pallas_call(
        body,
        grid_spec=grid_spec,
        out_shape=jax.ShapeDtypeStruct((count, sub, 128), pod_basis.dtype),
        compiler_params=pltpu.CompilerParams(dimension_semantics=("arbitrary",)),
    )(picks, pod_basis)


def block_products(jac_by_slot, table, column_slot):
    slots, rows, block_area = jac_by_slot.shape
    entries = table.shape[0]
    tile = ROW_TILE
    flat_slots = column_slot.T.reshape(-1)

    def body(col_ref, jac_ref, tab_ref, out_ref, part_ref, blocks_ref):
        step = pl.program_id(0)

        @pl.when(step == 0)
        def _():
            def relayout(c, carry):
                chunk = pl.ds(c * tile, tile)
                blocks_ref[chunk] = tab_ref[chunk].reshape(tile, BLOCK, MODES)
                return carry

            lax.fori_loop(0, entries // tile, relayout, 0)
            blocks_ref[entries] = jnp.zeros((BLOCK, MODES), blocks_ref.dtype)
            part_ref[...] = jnp.zeros_like(part_ref)

        acc = jnp.zeros((tile, BLOCK, MODES), jnp.float32)
        diag = None
        for j in range(slots):
            lhs = jac_ref[j].reshape(tile, BLOCK, BLOCK)
            picked = []
            for r in range(tile):
                e = col_ref[j * rows + step * tile + r]
                picked.append(blocks_ref[jnp.where(e >= 0, e, entries)])
            rhs = jnp.stack(picked)
            if j == 0:
                diag = rhs
            acc = acc + jnp.einsum(
                "rik,rkm->rim", lhs, rhs, preferred_element_type=jnp.float32
            )
        rounded = acc.astype(jnp.bfloat16)
        out_ref[...] = rounded.reshape(tile, block_area)
        part_ref[...] += lax.dot_general(
            diag.reshape(tile * BLOCK, MODES),
            rounded.reshape(tile * BLOCK, MODES),
            (((0,), (0,)), ((), ())),
            preferred_element_type=jnp.float32,
        )

    grid_spec = pltpu.PrefetchScalarGridSpec(
        num_scalar_prefetch=1,
        grid=(rows // tile,),
        in_specs=[
            pl.BlockSpec((slots, tile, block_area), lambda i, c: (0, i, 0)),
            pl.BlockSpec(table.shape, lambda i, c: (0, 0, 0)),
        ],
        out_specs=[
            pl.BlockSpec((tile, block_area), lambda i, c: (i, 0)),
            pl.BlockSpec((MODES, MODES), lambda i, c: (0, 0)),
        ],
        scratch_shapes=[pltpu.VMEM((entries + 1, BLOCK, MODES), table.dtype)],
    )
    return pl.pallas_call(
        body,
        grid_spec=grid_spec,
        out_shape=(
            jax.ShapeDtypeStruct((rows, block_area), jnp.bfloat16),
            jax.ShapeDtypeStruct((MODES, MODES), jnp.float32),
        ),
        compiler_params=pltpu.CompilerParams(dimension_semantics=("arbitrary",)),
    )(flat_slots, jac_by_slot, table)


def on_device(jacobian, pod_basis, ghost_rows, column_slot):
    rows_local = pod_basis.shape[0]
    dom_count = lax.axis_size("dom")
    outer_count = lax.axis_size("outer")
    device_count = dom_count * outer_count
    ghost_lists = ghost_rows[:, 0, :]
    ghost_count = ghost_lists.shape[1]
    outgoing = gather_outgoing(pod_basis, ghost_lists.T)
    outgoing = outgoing.reshape((device_count, ghost_count) + outgoing.shape[1:])
    received = lax.all_to_all(outgoing, ("dom", "outer"), split_axis=0, concat_axis=0, tiled=True)
    table = received.reshape((device_count * ghost_count,) + received.shape[2:])
    jac_by_slot = jnp.transpose(jacobian, (1, 0, 2))
    galerkin_rows, partial_value = block_products(jac_by_slot, table, column_slot)
    total = partial_value
    for stride, span in ((1, 2), (2, 4), (8, 4), (32, 4)):
        for flip in ((lambda d: 1 - d),) if span == 2 else ((lambda d: d ^ 1), (lambda d: 3 - d)):
            pairs = []
            for i in range(device_count):
                digit = (i // stride) % span
                pairs.append((i, i + (flip(digit) - digit) * stride))
            total = total + lax.ppermute(total, ("dom", "outer"), pairs)
    reduced = total / math.sqrt(rows_local * device_count * BLOCK)
    return (galerkin_rows, reduced)


def solution(mesh):
    placed = (
        P(("dom", "outer"), None, None),
        P(("dom", "outer"), None),
        P(None, ("dom", "outer"), None),
        P(("dom", "outer"), None),
    )
    return jax.shard_map(
        on_device,
        mesh=mesh,
        in_specs=placed,
        out_specs=(P(("dom", "outer"), None), P()),
        check_vma=False,
    )
```

```python
import math

import jax
import jax.numpy as jnp
from jax import lax
from jax.experimental import pallas as pl
from jax.experimental.pallas import tpu as pltpu
from jax.sharding import PartitionSpec as P

BLOCK = 64
MODES = 64
SLOTS = 7
ROW_TILE = 64
SEND_STEPS = 4


def gather_outgoing(pod_basis, picks_by_ghost):
    rows_local, block_area = pod_basis.shape
    ghosts, dests = picks_by_ghost.shape
    count = ghosts * dests
    picks = picks_by_ghost.reshape(-1)
    sub = block_area // 128

    per_step = count // SEND_STEPS
    dests_per_step = dests // SEND_STEPS

    def body(pick_ref, pod_ref, out_ref, slab_ref):
        step = pl.program_id(0)

        @pl.when(step == 0)
        def _():
            slab_ref[...] = pod_ref[...].reshape(rows_local, sub, 128)

        def one(dl, carry):
            d = step * dests_per_step + dl
            for g in range(ghosts):
                out_ref[dl * ghosts + g] = slab_ref[pick_ref[g * dests + d]]
            return carry

        lax.fori_loop(0, dests_per_step, one, 0, unroll=4)

    grid_spec = pltpu.PrefetchScalarGridSpec(
        num_scalar_prefetch=1,
        grid=(SEND_STEPS,),
        in_specs=[pl.BlockSpec((rows_local, block_area), lambda i, p: (0, 0))],
        out_specs=pl.BlockSpec((per_step, sub, 128), lambda i, p: (i, 0, 0)),
        scratch_shapes=[pltpu.VMEM((rows_local, sub, 128), pod_basis.dtype)],
    )
    return pl.pallas_call(
        body,
        grid_spec=grid_spec,
        out_shape=jax.ShapeDtypeStruct((count, sub, 128), pod_basis.dtype),
        compiler_params=pltpu.CompilerParams(dimension_semantics=("arbitrary",)),
    )(picks, pod_basis)


def block_products(jac_by_slot, table, column_slot):
    slots, rows, block_area = jac_by_slot.shape
    entries = table.shape[0]
    tile = ROW_TILE
    flat_slots = column_slot.T.reshape(-1)

    def body(col_ref, jac_ref, tab_ref, out_ref, part_ref, blocks_ref):
        step = pl.program_id(0)

        @pl.when(step == 0)
        def _():
            def relayout(c, carry):
                chunk = pl.ds(c * tile, tile)
                blocks_ref[chunk] = tab_ref[chunk].reshape(tile, BLOCK, MODES)
                return carry

            lax.fori_loop(0, entries // tile, relayout, 0)
            blocks_ref[entries] = jnp.zeros((BLOCK, MODES), blocks_ref.dtype)
            part_ref[...] = jnp.zeros_like(part_ref)

        acc = jnp.zeros((tile, BLOCK, MODES), jnp.float32)
        diag = None
        for j in range(slots):
            lhs = jac_ref[j].reshape(tile, BLOCK, BLOCK)
            picked = []
            for r in range(tile):
                e = col_ref[j * rows + step * tile + r]
                picked.append(blocks_ref[jnp.where(e >= 0, e, entries)])
            rhs = jnp.stack(picked)
            if j == 0:
                diag = rhs
            acc = acc + jnp.einsum(
                "rik,rkm->rim", lhs, rhs, preferred_element_type=jnp.float32
            )
        rounded = acc.astype(jnp.bfloat16)
        out_ref[...] = rounded.reshape(tile, block_area)
        part_ref[...] += lax.dot_general(
            diag.reshape(tile * BLOCK, MODES),
            rounded.reshape(tile * BLOCK, MODES),
            (((0,), (0,)), ((), ())),
            preferred_element_type=jnp.float32,
        )

    grid_spec = pltpu.PrefetchScalarGridSpec(
        num_scalar_prefetch=1,
        grid=(rows // tile,),
        in_specs=[
            pl.BlockSpec((slots, tile, block_area), lambda i, c: (0, i, 0)),
            pl.BlockSpec(table.shape, lambda i, c: (0, 0, 0)),
        ],
        out_specs=[
            pl.BlockSpec((tile, block_area), lambda i, c: (i, 0)),
            pl.BlockSpec((MODES, MODES), lambda i, c: (0, 0)),
        ],
        scratch_shapes=[pltpu.VMEM((entries + 1, BLOCK, MODES), table.dtype)],
    )
    return pl.pallas_call(
        body,
        grid_spec=grid_spec,
        out_shape=(
            jax.ShapeDtypeStruct((rows, block_area), jnp.bfloat16),
            jax.ShapeDtypeStruct((MODES, MODES), jnp.float32),
        ),
        compiler_params=pltpu.CompilerParams(dimension_semantics=("arbitrary",)),
    )(flat_slots, jac_by_slot, table)


def on_device(jacobian, pod_basis, ghost_rows, column_slot):
    rows_local = pod_basis.shape[0]
    dom_count = lax.axis_size("dom")
    outer_count = lax.axis_size("outer")
    device_count = dom_count * outer_count
    ghost_lists = ghost_rows[:, 0, :]
    ghost_count = ghost_lists.shape[1]
    outgoing = gather_outgoing(pod_basis, ghost_lists.T)
    outgoing = outgoing.reshape((device_count, ghost_count) + outgoing.shape[1:])
    received = lax.all_to_all(outgoing, ("dom", "outer"), split_axis=0, concat_axis=0, tiled=True)
    table = received.reshape((device_count * ghost_count,) + received.shape[2:])
    jac_by_slot = jnp.transpose(jacobian, (1, 0, 2))
    galerkin_rows, partial_value = block_products(jac_by_slot, table, column_slot)
    total = partial_value
    for stride, span in ((1, 2), (2, 4), (8, 4), (32, 4)):
        for flip in ((lambda d: 1 - d),) if span == 2 else ((lambda d: d ^ 1), (lambda d: 3 - d)):
            pairs = []
            for i in range(device_count):
                digit = (i // stride) % span
                pairs.append((i, i + (flip(digit) - digit) * stride))
            total = total + lax.ppermute(total, ("dom", "outer"), pairs)
    reduced = total / math.sqrt(rows_local * device_count * BLOCK)
    return (galerkin_rows, reduced)


def solution(mesh):
    placed = (
        P(("dom", "outer"), None, None),
        P(("dom", "outer"), None),
        P(None, ("dom", "outer"), None),
        P(("dom", "outer"), None),
    )
    return jax.shard_map(
        on_device,
        mesh=mesh,
        in_specs=placed,
        out_specs=(P(("dom", "outer"), None), P()),
        check_vma=False,
    )
```

```python
import math

import jax
import jax.numpy as jnp
from jax import lax
from jax.experimental import pallas as pl
from jax.experimental.pallas import tpu as pltpu
from jax.sharding import PartitionSpec as P

BLOCK = 64
MODES = 64
SLOTS = 7
ROW_TILE = 64
SEND_STEPS = 4


def gather_outgoing(pod_basis, picks_by_ghost):
    rows_local, block_area = pod_basis.shape
    ghosts, dests = picks_by_ghost.shape
    count = ghosts * dests
    picks = picks_by_ghost.reshape(-1)
    sub = block_area // 128

    per_step = count // SEND_STEPS
    dests_per_step = dests // SEND_STEPS

    def body(pick_ref, pod_ref, out_ref, slab_ref):
        step = pl.program_id(0)

        @pl.when(step == 0)
        def _():
            slab_ref[...] = pod_ref[...].reshape(rows_local, sub, 128)

        def one(dl, carry):
            d = step * dests_per_step + dl
            for g in range(ghosts):
                out_ref[dl * ghosts + g] = slab_ref[pick_ref[g * dests + d]]
            return carry

        lax.fori_loop(0, dests_per_step, one, 0, unroll=4)

    grid_spec = pltpu.PrefetchScalarGridSpec(
        num_scalar_prefetch=1,
        grid=(SEND_STEPS,),
        in_specs=[pl.BlockSpec((rows_local, block_area), lambda i, p: (0, 0))],
        out_specs=pl.BlockSpec((per_step, sub, 128), lambda i, p: (i, 0, 0)),
        scratch_shapes=[pltpu.VMEM((rows_local, sub, 128), pod_basis.dtype)],
    )
    return pl.pallas_call(
        body,
        grid_spec=grid_spec,
        out_shape=jax.ShapeDtypeStruct((count, sub, 128), pod_basis.dtype),
        compiler_params=pltpu.CompilerParams(dimension_semantics=("arbitrary",)),
    )(picks, pod_basis)


def relayout_jacobian(jac_by_slot):
    slots, rows, block_area = jac_by_slot.shape
    tile = ROW_TILE

    def body(jac_ref, out_ref):
        for j in range(slots):
            out_ref[j] = jac_ref[j].reshape(tile, BLOCK, BLOCK)

    return pl.pallas_call(
        body,
        grid=(rows // tile,),
        in_specs=[pl.BlockSpec((slots, tile, block_area), lambda i: (0, i, 0))],
        out_specs=pl.BlockSpec((slots, tile, BLOCK, BLOCK), lambda i: (0, i, 0, 0)),
        out_shape=jax.ShapeDtypeStruct((slots, rows, BLOCK, BLOCK), jac_by_slot.dtype),
    )(jac_by_slot)


def block_products(jac_by_slot, table, column_slot):
    slots, rows = jac_by_slot.shape[:2]
    block_area = BLOCK * MODES
    entries = table.shape[0]
    tile = ROW_TILE
    flat_slots = column_slot.T.reshape(-1)

    def body(col_ref, jac_ref, tab_ref, out_ref, part_ref, blocks_ref):
        step = pl.program_id(0)

        @pl.when(step == 0)
        def _():
            def relayout(c, carry):
                chunk = pl.ds(c * tile, tile)
                blocks_ref[chunk] = tab_ref[chunk].reshape(tile, BLOCK, MODES)
                return carry

            lax.fori_loop(0, entries // tile, relayout, 0)
            blocks_ref[entries] = jnp.zeros((BLOCK, MODES), blocks_ref.dtype)
            part_ref[...] = jnp.zeros_like(part_ref)

        acc = jnp.zeros((tile, BLOCK, MODES), jnp.float32)
        diag = None
        for j in range(slots):
            lhs = jac_ref[j]
            picked = []
            for r in range(tile):
                e = col_ref[j * rows + step * tile + r]
                picked.append(blocks_ref[jnp.where(e >= 0, e, entries)])
            rhs = jnp.stack(picked)
            if j == 0:
                diag = rhs
            acc = acc + jnp.einsum(
                "rik,rkm->rim", lhs, rhs, preferred_element_type=jnp.float32
            )
        rounded = acc.astype(jnp.bfloat16)
        out_ref[...] = rounded.reshape(tile, block_area)
        part_ref[...] += lax.dot_general(
            diag.reshape(tile * BLOCK, MODES),
            rounded.reshape(tile * BLOCK, MODES),
            (((0,), (0,)), ((), ())),
            preferred_element_type=jnp.float32,
        )

    grid_spec = pltpu.PrefetchScalarGridSpec(
        num_scalar_prefetch=1,
        grid=(rows // tile,),
        in_specs=[
            pl.BlockSpec((slots, tile, BLOCK, BLOCK), lambda i, c: (0, i, 0, 0)),
            pl.BlockSpec(table.shape, lambda i, c: (0, 0, 0)),
        ],
        out_specs=[
            pl.BlockSpec((tile, block_area), lambda i, c: (i, 0)),
            pl.BlockSpec((MODES, MODES), lambda i, c: (0, 0)),
        ],
        scratch_shapes=[pltpu.VMEM((entries + 1, BLOCK, MODES), table.dtype)],
    )
    return pl.pallas_call(
        body,
        grid_spec=grid_spec,
        out_shape=(
            jax.ShapeDtypeStruct((rows, block_area), jnp.bfloat16),
            jax.ShapeDtypeStruct((MODES, MODES), jnp.float32),
        ),
        compiler_params=pltpu.CompilerParams(dimension_semantics=("arbitrary",)),
    )(flat_slots, jac_by_slot, table)


def on_device(jacobian, pod_basis, ghost_rows, column_slot):
    rows_local = pod_basis.shape[0]
    dom_count = lax.axis_size("dom")
    outer_count = lax.axis_size("outer")
    device_count = dom_count * outer_count
    ghost_lists = ghost_rows[:, 0, :]
    ghost_count = ghost_lists.shape[1]
    outgoing = gather_outgoing(pod_basis, ghost_lists.T)
    outgoing = outgoing.reshape((device_count, ghost_count) + outgoing.shape[1:])
    received = lax.all_to_all(outgoing, ("dom", "outer"), split_axis=0, concat_axis=0, tiled=True)
    table = received.reshape((device_count * ghost_count,) + received.shape[2:])
    jac_by_slot = relayout_jacobian(jnp.transpose(jacobian, (1, 0, 2)))
    galerkin_rows, partial_value = block_products(jac_by_slot, table, column_slot)
    total = partial_value
    for stride, span in ((1, 2), (2, 4), (8, 4), (32, 4)):
        for flip in ((lambda d: 1 - d),) if span == 2 else ((lambda d: d ^ 1), (lambda d: 3 - d)):
            pairs = []
            for i in range(device_count):
                digit = (i // stride) % span
                pairs.append((i, i + (flip(digit) - digit) * stride))
            total = total + lax.ppermute(total, ("dom", "outer"), pairs)
    reduced = total / math.sqrt(rows_local * device_count * BLOCK)
    return (galerkin_rows, reduced)


def solution(mesh):
    placed = (
        P(("dom", "outer"), None, None),
        P(("dom", "outer"), None),
        P(None, ("dom", "outer"), None),
        P(("dom", "outer"), None),
    )
    return jax.shard_map(
        on_device,
        mesh=mesh,
        in_specs=placed,
        out_specs=(P(("dom", "outer"), None), P()),
        check_vma=False,
    )
```

```python
import math

import jax
import jax.numpy as jnp
from jax import lax
from jax.experimental import pallas as pl
from jax.experimental.pallas import tpu as pltpu
from jax.sharding import PartitionSpec as P

BLOCK = 64
MODES = 64
SLOTS = 7
ROW_TILE = 32
RELAYOUT_TILE = 64
SEND_STEPS = 4


def gather_outgoing(pod_basis, picks_by_ghost):
    rows_local, block_area = pod_basis.shape
    ghosts, dests = picks_by_ghost.shape
    count = ghosts * dests
    picks = picks_by_ghost.reshape(-1)
    sub = block_area // 128

    per_step = count // SEND_STEPS
    dests_per_step = dests // SEND_STEPS

    def body(pick_ref, pod_ref, out_ref, slab_ref):
        step = pl.program_id(0)

        @pl.when(step == 0)
        def _():
            slab_ref[...] = pod_ref[...].reshape(rows_local, sub, 128)

        def one(dl, carry):
            d = step * dests_per_step + dl
            for g in range(ghosts):
                out_ref[dl * ghosts + g] = slab_ref[pick_ref[g * dests + d]]
            return carry

        lax.fori_loop(0, dests_per_step, one, 0, unroll=4)

    grid_spec = pltpu.PrefetchScalarGridSpec(
        num_scalar_prefetch=1,
        grid=(SEND_STEPS,),
        in_specs=[pl.BlockSpec((rows_local, block_area), lambda i, p: (0, 0))],
        out_specs=pl.BlockSpec((per_step, sub, 128), lambda i, p: (i, 0, 0)),
        scratch_shapes=[pltpu.VMEM((rows_local, sub, 128), pod_basis.dtype)],
    )
    return pl.pallas_call(
        body,
        grid_spec=grid_spec,
        out_shape=jax.ShapeDtypeStruct((count, sub, 128), pod_basis.dtype),
        compiler_params=pltpu.CompilerParams(dimension_semantics=("arbitrary",)),
    )(picks, pod_basis)


def relayout_jacobian(jac_by_slot):
    slots, rows, block_area = jac_by_slot.shape
    tile = RELAYOUT_TILE

    def body(jac_ref, out_ref):
        for j in range(slots):
            out_ref[j] = jac_ref[j].reshape(tile, BLOCK, BLOCK)

    return pl.pallas_call(
        body,
        grid=(rows // tile,),
        in_specs=[pl.BlockSpec((slots, tile, block_area), lambda i: (0, i, 0))],
        out_specs=pl.BlockSpec((slots, tile, BLOCK, BLOCK), lambda i: (0, i, 0, 0)),
        out_shape=jax.ShapeDtypeStruct((slots, rows, BLOCK, BLOCK), jac_by_slot.dtype),
    )(jac_by_slot)


def block_products(jac_by_slot, table, column_slot):
    slots, rows = jac_by_slot.shape[:2]
    block_area = BLOCK * MODES
    entries = table.shape[0]
    tile = ROW_TILE
    flat_slots = column_slot.T.reshape(-1)

    def body(col_ref, jac_ref, tab_ref, out_ref, part_ref, blocks_ref):
        step = pl.program_id(0)

        @pl.when(step == 0)
        def _():
            def relayout(c, carry):
                chunk = pl.ds(c * tile, tile)
                blocks_ref[chunk] = tab_ref[chunk].reshape(tile, BLOCK, MODES)
                return carry

            lax.fori_loop(0, entries // tile, relayout, 0)
            blocks_ref[entries] = jnp.zeros((BLOCK, MODES), blocks_ref.dtype)
            part_ref[...] = jnp.zeros_like(part_ref)

        acc = jnp.zeros((tile, BLOCK, MODES), jnp.float32)
        diag = None
        for j in range(slots):
            lhs = jac_ref[j]
            picked = []
            for r in range(tile):
                e = col_ref[j * rows + step * tile + r]
                picked.append(blocks_ref[jnp.where(e >= 0, e, entries)])
            rhs = jnp.stack(picked)
            if j == 0:
                diag = rhs
            acc = acc + jnp.einsum(
                "rik,rkm->rim", lhs, rhs, preferred_element_type=jnp.float32
            )
        rounded = acc.astype(jnp.bfloat16)
        out_ref[...] = rounded.reshape(tile, block_area)
        part_ref[...] += lax.dot_general(
            diag.reshape(tile * BLOCK, MODES),
            rounded.reshape(tile * BLOCK, MODES),
            (((0,), (0,)), ((), ())),
            preferred_element_type=jnp.float32,
        )

    grid_spec = pltpu.PrefetchScalarGridSpec(
        num_scalar_prefetch=1,
        grid=(rows // tile,),
        in_specs=[
            pl.BlockSpec((slots, tile, BLOCK, BLOCK), lambda i, c: (0, i, 0, 0)),
            pl.BlockSpec(table.shape, lambda i, c: (0, 0, 0)),
        ],
        out_specs=[
            pl.BlockSpec((tile, block_area), lambda i, c: (i, 0)),
            pl.BlockSpec((MODES, MODES), lambda i, c: (0, 0)),
        ],
        scratch_shapes=[pltpu.VMEM((entries + 1, BLOCK, MODES), table.dtype)],
    )
    return pl.pallas_call(
        body,
        grid_spec=grid_spec,
        out_shape=(
            jax.ShapeDtypeStruct((rows, block_area), jnp.bfloat16),
            jax.ShapeDtypeStruct((MODES, MODES), jnp.float32),
        ),
        compiler_params=pltpu.CompilerParams(dimension_semantics=("arbitrary",)),
    )(flat_slots, jac_by_slot, table)


def on_device(jacobian, pod_basis, ghost_rows, column_slot):
    rows_local = pod_basis.shape[0]
    dom_count = lax.axis_size("dom")
    outer_count = lax.axis_size("outer")
    device_count = dom_count * outer_count
    ghost_lists = ghost_rows[:, 0, :]
    ghost_count = ghost_lists.shape[1]
    outgoing = gather_outgoing(pod_basis, ghost_lists.T)
    outgoing = outgoing.reshape((device_count, ghost_count) + outgoing.shape[1:])
    received = lax.all_to_all(outgoing, ("dom", "outer"), split_axis=0, concat_axis=0, tiled=True)
    table = received.reshape((device_count * ghost_count,) + received.shape[2:])
    jac_by_slot = relayout_jacobian(jnp.transpose(jacobian, (1, 0, 2)))
    galerkin_rows, partial_value = block_products(jac_by_slot, table, column_slot)
    total = partial_value
    for stride, span in ((1, 2), (2, 4), (8, 4), (32, 4)):
        for flip in ((lambda d: 1 - d),) if span == 2 else ((lambda d: d ^ 1), (lambda d: 3 - d)):
            pairs = []
            for i in range(device_count):
                digit = (i // stride) % span
                pairs.append((i, i + (flip(digit) - digit) * stride))
            total = total + lax.ppermute(total, ("dom", "outer"), pairs)
    reduced = total / math.sqrt(rows_local * device_count * BLOCK)
    return (galerkin_rows, reduced)


def solution(mesh):
    placed = (
        P(("dom", "outer"), None, None),
        P(("dom", "outer"), None),
        P(None, ("dom", "outer"), None),
        P(("dom", "outer"), None),
    )
    return jax.shard_map(
        on_device,
        mesh=mesh,
        in_specs=placed,
        out_specs=(P(("dom", "outer"), None), P()),
        check_vma=False,
    )
```

```python
import math

import jax
import jax.numpy as jnp
from jax import lax
from jax.experimental import pallas as pl
from jax.experimental.pallas import tpu as pltpu
from jax.sharding import PartitionSpec as P

BLOCK = 64
MODES = 64
SLOTS = 7
ROW_TILE = 64
SEND_STEPS = 8


def gather_outgoing(pod_basis, picks_by_ghost):
    rows_local, block_area = pod_basis.shape
    ghosts, dests = picks_by_ghost.shape
    count = ghosts * dests
    picks = picks_by_ghost.reshape(-1)
    sub = block_area // 128

    per_step = count // SEND_STEPS
    dests_per_step = dests // SEND_STEPS

    def body(pick_ref, pod_ref, out_ref, slab_ref):
        step = pl.program_id(0)

        @pl.when(step == 0)
        def _():
            slab_ref[...] = pod_ref[...].reshape(rows_local, sub, 128)

        def one(dl, carry):
            d = step * dests_per_step + dl
            for g in range(ghosts):
                out_ref[dl * ghosts + g] = slab_ref[pick_ref[g * dests + d]]
            return carry

        lax.fori_loop(0, dests_per_step, one, 0, unroll=4)

    grid_spec = pltpu.PrefetchScalarGridSpec(
        num_scalar_prefetch=1,
        grid=(SEND_STEPS,),
        in_specs=[pl.BlockSpec((rows_local, block_area), lambda i, p: (0, 0))],
        out_specs=pl.BlockSpec((per_step, sub, 128), lambda i, p: (i, 0, 0)),
        scratch_shapes=[pltpu.VMEM((rows_local, sub, 128), pod_basis.dtype)],
    )
    return pl.pallas_call(
        body,
        grid_spec=grid_spec,
        out_shape=jax.ShapeDtypeStruct((count, sub, 128), pod_basis.dtype),
        compiler_params=pltpu.CompilerParams(dimension_semantics=("arbitrary",)),
    )(picks, pod_basis)


def relayout_jacobian(jac_by_slot):
    slots, rows, block_area = jac_by_slot.shape
    tile = ROW_TILE

    def body(jac_ref, out_ref):
        for j in range(slots):
            out_ref[j] = jac_ref[j].reshape(tile, BLOCK, BLOCK)

    return pl.pallas_call(
        body,
        grid=(rows // tile,),
        in_specs=[pl.BlockSpec((slots, tile, block_area), lambda i: (0, i, 0))],
        out_specs=pl.BlockSpec((slots, tile, BLOCK, BLOCK), lambda i: (0, i, 0, 0)),
        out_shape=jax.ShapeDtypeStruct((slots, rows, BLOCK, BLOCK), jac_by_slot.dtype),
    )(jac_by_slot)


def block_products(jac_by_slot, table, column_slot):
    slots, rows = jac_by_slot.shape[:2]
    block_area = BLOCK * MODES
    entries = table.shape[0]
    tile = ROW_TILE
    flat_slots = column_slot.T.reshape(-1)

    def body(col_ref, jac_ref, tab_ref, out_ref, part_ref, blocks_ref):
        step = pl.program_id(0)

        @pl.when(step == 0)
        def _():
            def relayout(c, carry):
                chunk = pl.ds(c * tile, tile)
                blocks_ref[chunk] = tab_ref[chunk].reshape(tile, BLOCK, MODES)
                return carry

            lax.fori_loop(0, entries // tile, relayout, 0)
            blocks_ref[entries] = jnp.zeros((BLOCK, MODES), blocks_ref.dtype)
            part_ref[...] = jnp.zeros_like(part_ref)

        acc = jnp.zeros((tile, BLOCK, MODES), jnp.float32)
        diag = None
        for j in range(slots):
            lhs = jac_ref[j]
            picked = []
            for r in range(tile):
                e = col_ref[j * rows + step * tile + r]
                picked.append(blocks_ref[jnp.where(e >= 0, e, entries)])
            rhs = jnp.stack(picked)
            if j == 0:
                diag = rhs
            acc = acc + jnp.einsum(
                "rik,rkm->rim", lhs, rhs, preferred_element_type=jnp.float32
            )
        rounded = acc.astype(jnp.bfloat16)
        out_ref[...] = rounded.reshape(tile, block_area)
        part_ref[...] += lax.dot_general(
            diag.reshape(tile * BLOCK, MODES),
            rounded.reshape(tile * BLOCK, MODES),
            (((0,), (0,)), ((), ())),
            preferred_element_type=jnp.float32,
        )

    grid_spec = pltpu.PrefetchScalarGridSpec(
        num_scalar_prefetch=1,
        grid=(rows // tile,),
        in_specs=[
            pl.BlockSpec((slots, tile, BLOCK, BLOCK), lambda i, c: (0, i, 0, 0)),
            pl.BlockSpec(table.shape, lambda i, c: (0, 0, 0)),
        ],
        out_specs=[
            pl.BlockSpec((tile, block_area), lambda i, c: (i, 0)),
            pl.BlockSpec((MODES, MODES), lambda i, c: (0, 0)),
        ],
        scratch_shapes=[pltpu.VMEM((entries + 1, BLOCK, MODES), table.dtype)],
    )
    return pl.pallas_call(
        body,
        grid_spec=grid_spec,
        out_shape=(
            jax.ShapeDtypeStruct((rows, block_area), jnp.bfloat16),
            jax.ShapeDtypeStruct((MODES, MODES), jnp.float32),
        ),
        compiler_params=pltpu.CompilerParams(dimension_semantics=("arbitrary",)),
    )(flat_slots, jac_by_slot, table)


def on_device(jacobian, pod_basis, ghost_rows, column_slot):
    rows_local = pod_basis.shape[0]
    dom_count = lax.axis_size("dom")
    outer_count = lax.axis_size("outer")
    device_count = dom_count * outer_count
    ghost_lists = ghost_rows[:, 0, :]
    ghost_count = ghost_lists.shape[1]
    outgoing = gather_outgoing(pod_basis, ghost_lists.T)
    outgoing = outgoing.reshape((device_count, ghost_count) + outgoing.shape[1:])
    received = lax.all_to_all(outgoing, ("dom", "outer"), split_axis=0, concat_axis=0, tiled=True)
    table = received.reshape((device_count * ghost_count,) + received.shape[2:])
    jac_by_slot = relayout_jacobian(jnp.transpose(jacobian, (1, 0, 2)))
    galerkin_rows, partial_value = block_products(jac_by_slot, table, column_slot)
    total = partial_value
    for stride, span in ((1, 2), (2, 4), (8, 4), (32, 4)):
        for flip in ((lambda d: 1 - d),) if span == 2 else ((lambda d: d ^ 1), (lambda d: 3 - d)):
            pairs = []
            for i in range(device_count):
                digit = (i // stride) % span
                pairs.append((i, i + (flip(digit) - digit) * stride))
            total = total + lax.ppermute(total, ("dom", "outer"), pairs)
    reduced = total / math.sqrt(rows_local * device_count * BLOCK)
    return (galerkin_rows, reduced)


def solution(mesh):
    placed = (
        P(("dom", "outer"), None, None),
        P(("dom", "outer"), None),
        P(None, ("dom", "outer"), None),
        P(("dom", "outer"), None),
    )
    return jax.shard_map(
        on_device,
        mesh=mesh,
        in_specs=placed,
        out_specs=(P(("dom", "outer"), None), P()),
        check_vma=False,
    )
```

```python
import math

import jax
import jax.numpy as jnp
from jax import lax
from jax.experimental import pallas as pl
from jax.experimental.pallas import tpu as pltpu
from jax.sharding import PartitionSpec as P

BLOCK = 64
MODES = 64
SLOTS = 7
ROW_TILE = 64
SEND_STEPS = 4


def gather_outgoing(pod_basis, picks_by_ghost):
    rows_local, block_area = pod_basis.shape
    ghosts, dests = picks_by_ghost.shape
    count = ghosts * dests
    picks = picks_by_ghost.reshape(-1)
    sub = block_area // 128

    per_step = count // SEND_STEPS
    dests_per_step = dests // SEND_STEPS

    def body(pick_ref, pod_ref, out_ref, slab_ref):
        step = pl.program_id(0)

        @pl.when(step == 0)
        def _():
            slab_ref[...] = pod_ref[...].reshape(rows_local, sub, 128)

        def one(dl, carry):
            d = step * dests_per_step + dl
            for g in range(ghosts):
                out_ref[dl * ghosts + g] = slab_ref[pick_ref[g * dests + d]]
            return carry

        lax.fori_loop(0, dests_per_step, one, 0, unroll=4)

    grid_spec = pltpu.PrefetchScalarGridSpec(
        num_scalar_prefetch=1,
        grid=(SEND_STEPS,),
        in_specs=[pl.BlockSpec((rows_local, block_area), lambda i, p: (0, 0))],
        out_specs=pl.BlockSpec((per_step, sub, 128), lambda i, p: (i, 0, 0)),
        scratch_shapes=[pltpu.VMEM((rows_local, sub, 128), pod_basis.dtype)],
    )
    return pl.pallas_call(
        body,
        grid_spec=grid_spec,
        out_shape=jax.ShapeDtypeStruct((count, sub, 128), pod_basis.dtype),
        compiler_params=pltpu.CompilerParams(dimension_semantics=("arbitrary",)),
    )(picks, pod_basis)


def relayout_jacobian(jac_by_slot):
    slots, rows, block_area = jac_by_slot.shape
    tile = ROW_TILE

    def body(jac_ref, out_ref):
        for j in range(slots):
            out_ref[j] = jac_ref[j].reshape(tile, BLOCK, BLOCK)

    return pl.pallas_call(
        body,
        grid=(rows // tile,),
        in_specs=[pl.BlockSpec((slots, tile, block_area), lambda i: (0, i, 0))],
        out_specs=pl.BlockSpec((slots, tile, BLOCK, BLOCK), lambda i: (0, i, 0, 0)),
        out_shape=jax.ShapeDtypeStruct((slots, rows, BLOCK, BLOCK), jac_by_slot.dtype),
    )(jac_by_slot)


def block_products(jac_by_slot, table, column_slot, scale):
    slots, rows = jac_by_slot.shape[:2]
    block_area = BLOCK * MODES
    entries = table.shape[0]
    tile = ROW_TILE
    flat_slots = column_slot.T.reshape(-1)

    def body(col_ref, jac_ref, tab_ref, out_ref, part_ref, blocks_ref):
        step = pl.program_id(0)

        @pl.when(step == 0)
        def _():
            def relayout(c, carry):
                chunk = pl.ds(c * tile, tile)
                blocks_ref[chunk] = tab_ref[chunk].reshape(tile, BLOCK, MODES)
                return carry

            lax.fori_loop(0, entries // tile, relayout, 0)
            blocks_ref[entries] = jnp.zeros((BLOCK, MODES), blocks_ref.dtype)
            part_ref[...] = jnp.zeros_like(part_ref)

        acc = jnp.zeros((tile, BLOCK, MODES), jnp.float32)
        diag = None
        for j in range(slots):
            lhs = jac_ref[j]
            picked = []
            for r in range(tile):
                e = col_ref[j * rows + step * tile + r]
                picked.append(blocks_ref[jnp.where(e >= 0, e, entries)])
            rhs = jnp.stack(picked)
            if j == 0:
                diag = rhs
            acc = acc + jnp.einsum(
                "rik,rkm->rim", lhs, rhs, preferred_element_type=jnp.float32
            )
        rounded = acc.astype(jnp.bfloat16)
        out_ref[...] = rounded.reshape(tile, block_area)
        part_ref[...] += scale * lax.dot_general(
            diag.reshape(tile * BLOCK, MODES),
            rounded.reshape(tile * BLOCK, MODES),
            (((0,), (0,)), ((), ())),
            preferred_element_type=jnp.float32,
        )

    grid_spec = pltpu.PrefetchScalarGridSpec(
        num_scalar_prefetch=1,
        grid=(rows // tile,),
        in_specs=[
            pl.BlockSpec((slots, tile, BLOCK, BLOCK), lambda i, c: (0, i, 0, 0)),
            pl.BlockSpec(table.shape, lambda i, c: (0, 0, 0)),
        ],
        out_specs=[
            pl.BlockSpec((tile, block_area), lambda i, c: (i, 0)),
            pl.BlockSpec((MODES, MODES), lambda i, c: (0, 0)),
        ],
        scratch_shapes=[pltpu.VMEM((entries + 1, BLOCK, MODES), table.dtype)],
    )
    return pl.pallas_call(
        body,
        grid_spec=grid_spec,
        out_shape=(
            jax.ShapeDtypeStruct((rows, block_area), jnp.bfloat16),
            jax.ShapeDtypeStruct((MODES, MODES), jnp.float32),
        ),
        compiler_params=pltpu.CompilerParams(dimension_semantics=("arbitrary",)),
    )(flat_slots, jac_by_slot, table)


def on_device(jacobian, pod_basis, ghost_rows, column_slot):
    rows_local = pod_basis.shape[0]
    dom_count = lax.axis_size("dom")
    outer_count = lax.axis_size("outer")
    device_count = dom_count * outer_count
    ghost_lists = ghost_rows[:, 0, :]
    ghost_count = ghost_lists.shape[1]
    outgoing = gather_outgoing(pod_basis, ghost_lists.T)
    outgoing = outgoing.reshape((device_count, ghost_count) + outgoing.shape[1:])
    received = lax.all_to_all(outgoing, ("dom", "outer"), split_axis=0, concat_axis=0, tiled=True)
    table = received.reshape((device_count * ghost_count,) + received.shape[2:])
    jac_by_slot = relayout_jacobian(jnp.transpose(jacobian, (1, 0, 2)))
    scale = 1.0 / math.sqrt(rows_local * device_count * BLOCK)
    galerkin_rows, partial_value = block_products(jac_by_slot, table, column_slot, scale)
    total = partial_value
    for stride, span in ((1, 2), (2, 4), (8, 4), (32, 4)):
        for flip in ((lambda d: 1 - d),) if span == 2 else ((lambda d: d ^ 1), (lambda d: 3 - d)):
            pairs = []
            for i in range(device_count):
                digit = (i // stride) % span
                pairs.append((i, i + (flip(digit) - digit) * stride))
            total = total + lax.ppermute(total, ("dom", "outer"), pairs)
    reduced = total
    return (galerkin_rows, reduced)


def solution(mesh):
    placed = (
        P(("dom", "outer"), None, None),
        P(("dom", "outer"), None),
        P(None, ("dom", "outer"), None),
        P(("dom", "outer"), None),
    )
    return jax.shard_map(
        on_device,
        mesh=mesh,
        in_specs=placed,
        out_specs=(P(("dom", "outer"), None), P()),
        check_vma=False,
    )
```

```python
import math

import jax
import jax.numpy as jnp
from jax import lax
from jax.experimental import pallas as pl
from jax.experimental.pallas import tpu as pltpu
from jax.sharding import PartitionSpec as P

BLOCK = 64
MODES = 64
SLOTS = 7
ROW_TILE = 64
SEND_STEPS = 4


def gather_outgoing(pod_basis, picks_by_ghost):
    rows_local, block_area = pod_basis.shape
    ghosts, dests = picks_by_ghost.shape
    count = ghosts * dests
    picks = picks_by_ghost.reshape(-1)
    sub = block_area // 128

    per_step = count // SEND_STEPS
    dests_per_step = dests // SEND_STEPS

    def body(pick_ref, pod_ref, out_ref, slab_ref):
        step = pl.program_id(0)

        @pl.when(step == 0)
        def _():
            slab_ref[...] = pod_ref[...].reshape(rows_local, sub, 128)

        def one(dl, carry):
            d = step * dests_per_step + dl
            for g in range(ghosts):
                out_ref[dl * ghosts + g] = slab_ref[pick_ref[g * dests + d]]
            return carry

        lax.fori_loop(0, dests_per_step, one, 0, unroll=8)

    grid_spec = pltpu.PrefetchScalarGridSpec(
        num_scalar_prefetch=1,
        grid=(SEND_STEPS,),
        in_specs=[pl.BlockSpec((rows_local, block_area), lambda i, p: (0, 0))],
        out_specs=pl.BlockSpec((per_step, sub, 128), lambda i, p: (i, 0, 0)),
        scratch_shapes=[pltpu.VMEM((rows_local, sub, 128), pod_basis.dtype)],
    )
    return pl.pallas_call(
        body,
        grid_spec=grid_spec,
        out_shape=jax.ShapeDtypeStruct((count, sub, 128), pod_basis.dtype),
        compiler_params=pltpu.CompilerParams(dimension_semantics=("arbitrary",)),
    )(picks, pod_basis)


def relayout_jacobian(jac_by_slot):
    slots, rows, block_area = jac_by_slot.shape
    tile = ROW_TILE

    def body(jac_ref, out_ref):
        for j in range(slots):
            out_ref[j] = jac_ref[j].reshape(tile, BLOCK, BLOCK)

    return pl.pallas_call(
        body,
        grid=(rows // tile,),
        in_specs=[pl.BlockSpec((slots, tile, block_area), lambda i: (0, i, 0))],
        out_specs=pl.BlockSpec((slots, tile, BLOCK, BLOCK), lambda i: (0, i, 0, 0)),
        out_shape=jax.ShapeDtypeStruct((slots, rows, BLOCK, BLOCK), jac_by_slot.dtype),
    )(jac_by_slot)


def block_products(jac_by_slot, table, column_slot, scale):
    slots, rows = jac_by_slot.shape[:2]
    block_area = BLOCK * MODES
    entries = table.shape[0]
    tile = ROW_TILE
    flat_slots = column_slot.T.reshape(-1)

    def body(col_ref, jac_ref, tab_ref, out_ref, part_ref, blocks_ref):
        step = pl.program_id(0)

        @pl.when(step == 0)
        def _():
            def relayout(c, carry):
                chunk = pl.ds(c * tile, tile)
                blocks_ref[chunk] = tab_ref[chunk].reshape(tile, BLOCK, MODES)
                return carry

            lax.fori_loop(0, entries // tile, relayout, 0)
            blocks_ref[entries] = jnp.zeros((BLOCK, MODES), blocks_ref.dtype)
            part_ref[...] = jnp.zeros_like(part_ref)

        acc = jnp.zeros((tile, BLOCK, MODES), jnp.float32)
        diag = None
        for j in range(slots):
            lhs = jac_ref[j]
            picked = []
            for r in range(tile):
                e = col_ref[j * rows + step * tile + r]
                picked.append(blocks_ref[jnp.where(e >= 0, e, entries)])
            rhs = jnp.stack(picked)
            if j == 0:
                diag = rhs
            acc = acc + jnp.einsum(
                "rik,rkm->rim", lhs, rhs, preferred_element_type=jnp.float32
            )
        rounded = acc.astype(jnp.bfloat16)
        out_ref[...] = rounded.reshape(tile, block_area)
        part_ref[...] += scale * lax.dot_general(
            diag.reshape(tile * BLOCK, MODES),
            rounded.reshape(tile * BLOCK, MODES),
            (((0,), (0,)), ((), ())),
            preferred_element_type=jnp.float32,
        )

    grid_spec = pltpu.PrefetchScalarGridSpec(
        num_scalar_prefetch=1,
        grid=(rows // tile,),
        in_specs=[
            pl.BlockSpec((slots, tile, BLOCK, BLOCK), lambda i, c: (0, i, 0, 0)),
            pl.BlockSpec(table.shape, lambda i, c: (0, 0, 0)),
        ],
        out_specs=[
            pl.BlockSpec((tile, block_area), lambda i, c: (i, 0)),
            pl.BlockSpec((MODES, MODES), lambda i, c: (0, 0)),
        ],
        scratch_shapes=[pltpu.VMEM((entries + 1, BLOCK, MODES), table.dtype)],
    )
    return pl.pallas_call(
        body,
        grid_spec=grid_spec,
        out_shape=(
            jax.ShapeDtypeStruct((rows, block_area), jnp.bfloat16),
            jax.ShapeDtypeStruct((MODES, MODES), jnp.float32),
        ),
        compiler_params=pltpu.CompilerParams(dimension_semantics=("arbitrary",)),
    )(flat_slots, jac_by_slot, table)


def on_device(jacobian, pod_basis, ghost_rows, column_slot):
    rows_local = pod_basis.shape[0]
    dom_count = lax.axis_size("dom")
    outer_count = lax.axis_size("outer")
    device_count = dom_count * outer_count
    ghost_lists = ghost_rows[:, 0, :]
    ghost_count = ghost_lists.shape[1]
    outgoing = gather_outgoing(pod_basis, ghost_lists.T)
    outgoing = outgoing.reshape((device_count, ghost_count) + outgoing.shape[1:])
    received = lax.all_to_all(outgoing, ("dom", "outer"), split_axis=0, concat_axis=0, tiled=True)
    table = received.reshape((device_count * ghost_count,) + received.shape[2:])
    jac_by_slot = relayout_jacobian(jnp.transpose(jacobian, (1, 0, 2)))
    scale = 1.0 / math.sqrt(rows_local * device_count * BLOCK)
    galerkin_rows, partial_value = block_products(jac_by_slot, table, column_slot, scale)
    total = partial_value
    for stride, span in ((1, 2), (2, 4), (8, 4), (32, 4)):
        for flip in ((lambda d: 1 - d),) if span == 2 else ((lambda d: d ^ 1), (lambda d: 3 - d)):
            pairs = []
            for i in range(device_count):
                digit = (i // stride) % span
                pairs.append((i, i + (flip(digit) - digit) * stride))
            total = total + lax.ppermute(total, ("dom", "outer"), pairs)
    reduced = total
    return (galerkin_rows, reduced)


def solution(mesh):
    placed = (
        P(("dom", "outer"), None, None),
        P(("dom", "outer"), None),
        P(None, ("dom", "outer"), None),
        P(("dom", "outer"), None),
    )
    return jax.shard_map(
        on_device,
        mesh=mesh,
        in_specs=placed,
        out_specs=(P(("dom", "outer"), None), P()),
        check_vma=False,
    )
```
